512 devices in a mesh: sub: 64 (over x, z), grp: 8 (over y, core).
Axes of the slice: x: 4, y: 4, z: 16, core: 2. Of those that a mesh axis runs over, the one named last changes fastest.
Arguments:
- tiles: bfloat16 [8, 4096, 128, 128], P('grp', 'sub'), may hold values from -6 to 6
- dest_owner: int32 [8, 4096], P('grp', 'sub'), may hold values from 0 to 63, as said below
- dest_slot: int32 [8, 4096], P('grp', 'sub'), may hold values from 0 to 7
- triples: int32 [3, 1024], replicated, may hold values from 130 to 4030, as said below
Outputs:
- bispectrum: float32 [512, 2, 1024], P('sub', None, 'grp')
The draws below stay inside these ranges and needn't reach their ends.
Inputs may be any that keep to these rules, and one draw needn't show every extreme that they name: `dest_owner`: in each frame group, among the 64 tile frames of one index of sub, no owner is named more than 2 times; in each frame group one owner is named exactly 2 times by every index of sub. `triples`: each column holds the flat indices (a + 32) * 64 + (b + 32) of frequencies (a, b) = u, v and u + v.
All inputs are finite; a program needn't handle non-finite values.
Results may differ from the reference program's by a relative error of at most 0.012.
Values may be sent and summed in bfloat16 or wider, within the bound.
No kernel may reach another device: no remote copies, remote signals or barrier semaphores. Data moves between devices by JAX's collectives and lax.ppermute only.
A program may use at most 64 MiB of HBM per device.

```python
import math
import jax
import jax.numpy as jnp
from jax import lax

PATCH = 128
BOX = 64
OWN = 8
TILES_DEV = 64
GROUPS = 8
NTRI = 1024
N_SUB = 64


def draw_dest_owner(key, part):
    capacity = 2 * TILES_DEV // N_SUB
    key_hot, key_pop, key_blocks = jax.random.split(key, 3)
    hot = jax.random.randint(key_hot, (GROUPS,), 0, N_SUB)
    popular = jax.random.randint(key_pop, (GROUPS, N_SUB), 0, 4)

    def one_block(block_key, hot_owner, weights):
        others = (hot_owner + 1 + jnp.arange(N_SUB - 1, dtype=jnp.int32)) % N_SUB
        candidates = jnp.repeat(others, capacity)
        length = candidates.shape[0]
        key_score, key_perm = jax.random.split(block_key)
        score = jax.random.randint(key_score, (length,), 0, 64) + 64 * weights[candidates]
        score = score * length + jnp.arange(length, dtype=jnp.int32)
        order = jnp.argsort(-score)
        chosen = candidates[order[:TILES_DEV - capacity]]
        whole = jnp.concatenate([jnp.full((capacity,), hot_owner, jnp.int32), chosen.astype(jnp.int32)])
        return jax.random.permutation(key_perm, whole)
    block_keys = jax.random.split(key_blocks, GROUPS * N_SUB)
    hot_rep = jnp.repeat(hot, N_SUB)
    pop_rep = jnp.repeat(popular, N_SUB, axis=0)
    blocks = jax.vmap(one_block)(block_keys, hot_rep, pop_rep)
    return blocks.reshape(GROUPS, N_SUB * TILES_DEV).astype(jnp.int32)


def draw_triples(key, part):
    centre = BOX // 2
    reach = centre // 2 - 1
    keys = jax.random.split(key, 4)
    first_a = jax.random.randint(keys[0], (NTRI,), -reach, reach + 1)
    first_b = jax.random.randint(keys[1], (NTRI,), -reach, reach + 1)
    second_a = jax.random.randint(keys[2], (NTRI,), -reach, reach + 1)
    second_b = jax.random.randint(keys[3], (NTRI,), -reach, reach + 1)

    def flat_index(row_freq, col_freq):
        return (row_freq + centre) * BOX + (col_freq + centre)
    return jnp.stack([flat_index(first_a, first_b), flat_index(second_a, second_b), flat_index(first_a + second_a, first_b + second_b)]).astype(jnp.int32)


def set_ends(drawn, rng, low, largest):
    longest = drawn.shape.index(max(drawn.shape))
    spots = []
    for shift in (0, 1):
        where = [jax.random.randint(jax.random.fold_in(rng, axis), (), 0, length) for axis, length in enumerate(drawn.shape)]
        where[longest] = (where[longest] + shift) % drawn.shape[longest]
        spots.append(tuple(where))
    return drawn.at[spots[0]].set(low).at[spots[1]].set(largest)


def steps_of(rng, extent, cuts, low, top_value):
    def one(position, parts):
        steps = jax.random.uniform(jax.random.fold_in(jax.random.fold_in(rng, 6), position), (parts,), jnp.float32, low / len(cuts), top_value / len(cuts))
        return jnp.repeat(jnp.exp(steps), extent[position] // parts).reshape((-1,) + (1,) * (len(extent) - position - 1))

    loudness = one(*cuts[0])
    for cut in cuts[1:]:
        loudness = loudness * one(*cut)
    return loudness


def bell_draw(key, shape, width, limit, shards=(), kind=jnp.bfloat16):
    entries = width * jax.random.normal(key, shape, jnp.float32)
    if shards:
        entries = entries * steps_of(key, shape, shards, -0.22, 0.18)
    return jnp.clip(entries, -limit, limit).astype(kind)


def setup_inputs(seed: int = 0) -> dict:
    key_of = jax.random.split(jax.random.key(seed), 5)
    tiles = bell_draw(key_of[0], (GROUPS, N_SUB * TILES_DEV, PATCH, PATCH), 1.0, 6.0, ((0, 8), (1, 64)))
    dest_owner = draw_dest_owner(jax.random.fold_in(key_of[4], 71), 0)
    dest_slot = set_ends(jax.random.randint(key_of[2], (GROUPS, N_SUB * TILES_DEV), 0, OWN), jax.random.fold_in(key_of[2], 1), 0, OWN - 1).astype(jnp.int32)
    triples = draw_triples(jax.random.fold_in(key_of[4], 71), 0)
    return {"tiles": tiles, "dest_owner": dest_owner, "dest_slot": dest_slot, "triples": triples}


def make_tables(patch, box):
    rows = jnp.arange(patch, dtype=jnp.int32)[:, None]
    cols = jnp.arange(box, dtype=jnp.int32)[None, :] - box // 2 + patch
    phase = rows * cols % patch
    angle = 2.0 * math.pi * phase.astype(jnp.float32) / patch
    scale = 1.0 / math.sqrt(patch)
    cos_tab = (jnp.cos(angle) * scale).astype(jnp.bfloat16)
    sin_tab = (-jnp.sin(angle) * scale).astype(jnp.bfloat16)
    centre = (jnp.arange(patch, dtype=jnp.float32) + 0.5) / patch
    hann = 0.5 - 0.5 * jnp.cos(2.0 * math.pi * centre)
    window = hann[:, None] * hann[None, :]
    return (cos_tab, sin_tab, window)

def spectra_of(block, cos_tab, sin_tab, window):
    box = cos_tab.shape[1]
    apodised = (block.astype(jnp.float32) * window).astype(jnp.bfloat16)
    right = jnp.concatenate([cos_tab, sin_tab], axis=1).astype(jnp.float32)
    half = jnp.einsum('nij,jc->nic', apodised.astype(jnp.float32), right, precision=lax.Precision.HIGHEST).astype(jnp.bfloat16)
    left = jnp.concatenate([cos_tab.T, sin_tab.T], axis=0).astype(jnp.float32)
    full = jnp.einsum('ki,nic->nkc', left, half.astype(jnp.float32), precision=lax.Precision.HIGHEST)
    real_part = full[:, :box, :box] - full[:, box:, box:]
    imag_part = full[:, :box, box:] + full[:, box:, :box]
    count = block.shape[0]
    return jnp.stack([real_part, imag_part], axis=1).reshape(count, 2, box * box).astype(jnp.bfloat16)

def triple_terms(spectrum, triples):
    first = jnp.take(spectrum, triples[0], axis=2).astype(jnp.float32)
    second = jnp.take(spectrum, triples[1], axis=2).astype(jnp.float32)
    third = jnp.take(spectrum, triples[2], axis=2).astype(jnp.float32)
    prod_real = first[:, 0] * second[:, 0] - first[:, 1] * second[:, 1]
    prod_imag = first[:, 0] * second[:, 1] + first[:, 1] * second[:, 0]
    out_real = prod_real * third[:, 0] + prod_imag * third[:, 1]
    out_imag = prod_imag * third[:, 0] - prod_real * third[:, 1]
    return jnp.stack([out_real, out_imag], axis=1)

def reference(tiles, dest_owner, dest_slot, triples):
    cos_tab, sin_tab, window = make_tables(PATCH, BOX)
    total = GROUPS * N_SUB * TILES_DEV
    block_len = math.gcd(total, 256)
    flat_tiles = tiles.reshape(total // block_len, block_len, PATCH, PATCH)
    target = (dest_owner * OWN + dest_slot).astype(jnp.int32).reshape(total // block_len, block_len)

    def step(carry, inputs):
        block, where = inputs
        spectrum = spectra_of(block, cos_tab, sin_tab, window)
        terms = triple_terms(spectrum, triples)
        return (carry + jax.ops.segment_sum(terms, where, num_segments=N_SUB * OWN), None)
    start = jnp.zeros((N_SUB * OWN, 2, NTRI), jnp.float32)
    result, unused = lax.scan(step, start, (flat_tiles, target))
    return result
```

```python
import math

import jax
import jax.numpy as jnp
from jax import lax
from jax.sharding import PartitionSpec as P

BOX = 64
OWN = 8


def make_tables(patch, box):
    rows = jnp.arange(patch, dtype=jnp.int32)[:, None]
    cols = jnp.arange(box, dtype=jnp.int32)[None, :] - box // 2 + patch
    phase = rows * cols % patch
    angle = 2.0 * math.pi * phase.astype(jnp.float32) / patch
    scale = 1.0 / math.sqrt(patch)
    cos_tab = (jnp.cos(angle) * scale).astype(jnp.bfloat16)
    sin_tab = (-jnp.sin(angle) * scale).astype(jnp.bfloat16)
    centre = (jnp.arange(patch, dtype=jnp.float32) + 0.5) / patch
    hann = 0.5 - 0.5 * jnp.cos(2.0 * math.pi * centre)
    window = hann[:, None] * hann[None, :]
    right = jnp.concatenate([cos_tab, sin_tab], axis=1)
    left = jnp.transpose(right)
    return (right, left, window)


def spectra_freq_major(frames, right, left, window):
    box = right.shape[1] // 2
    count = frames.shape[0]
    apodised = (frames.astype(jnp.float32) * window).astype(jnp.bfloat16)
    half = jnp.einsum("nij,jc->nic", apodised, right, preferred_element_type=jnp.float32).astype(
        jnp.bfloat16
    )
    full = jnp.einsum("ki,nic->kcn", left, half, preferred_element_type=jnp.float32)
    real_part = full[:box, :box] - full[box:, box:]
    imag_part = full[:box, box:] + full[box:, :box]
    spec = jnp.stack([real_part, imag_part], axis=2).astype(jnp.bfloat16)
    return spec.reshape(box * box, 2 * count)


def local(tiles, dest_owner, dest_slot, triples):
    frames = tiles[0]
    count = frames.shape[0]
    patch = frames.shape[-1]
    groups = lax.axis_size("grp")
    peers = lax.axis_size("sub")
    target = dest_owner[0] * OWN + dest_slot[0]
    right, left, window = make_tables(patch, BOX)
    spec = spectra_freq_major(frames, right, left, window)
    picked = [jnp.take(spec, triples[w], axis=0).astype(jnp.float32) for w in range(3)]
    ntri = triples.shape[1]
    first, second, third = [p.reshape(ntri, 2, count) for p in picked]
    prod_real = first[:, 0] * second[:, 0] - first[:, 1] * second[:, 1]
    prod_imag = first[:, 0] * second[:, 1] + first[:, 1] * second[:, 0]
    out_real = prod_real * third[:, 0] + prod_imag * third[:, 1]
    out_imag = prod_imag * third[:, 0] - prod_real * third[:, 1]
    terms = jnp.stack([out_real, out_imag], axis=1)
    block = ntri // groups
    terms = terms.reshape(groups, block, 2, count)
    marks = jnp.broadcast_to(target.astype(jnp.float32)[None, None, None, :], (groups, 8, 2, count))
    payload = jnp.concatenate([terms, marks], axis=1)
    got = lax.all_to_all(payload, "grp", split_axis=0, concat_axis=0, tiled=True)
    got_terms = got[:, :block]
    got_marks = got[:, block, 0, :].astype(jnp.int32)
    rows = peers * OWN
    onehot = (
        got_marks[None, :, :] == jnp.arange(rows, dtype=jnp.int32)[:, None, None]
    ).astype(jnp.float32)
    partial_value = jnp.einsum(
        "rgn,gtcn->rct", onehot, got_terms, precision=lax.Precision.HIGHEST
    )
    return lax.psum_scatter(partial_value, "sub", scatter_dimension=0, tiled=True)


def solution(mesh):
    in_specs = (P("grp", "sub", None, None), P("grp", "sub"), P("grp", "sub"), P())
    out_specs = P("sub", None, "grp")
    return jax.shard_map(local, mesh=mesh, in_specs=in_specs, out_specs=out_specs, check_vma=False)
```

```python
import math

import jax
import jax.numpy as jnp
from jax import lax
from jax.sharding import PartitionSpec as P

BOX = 64
OWN = 8


def make_tables(patch, box):
    rows = jnp.arange(patch, dtype=jnp.int32)[:, None]
    cols = jnp.arange(box, dtype=jnp.int32)[None, :] - box // 2 + patch
    phase = rows * cols % patch
    angle = 2.0 * math.pi * phase.astype(jnp.float32) / patch
    scale = 1.0 / math.sqrt(patch)
    cos_tab = (jnp.cos(angle) * scale).astype(jnp.bfloat16)
    sin_tab = (-jnp.sin(angle) * scale).astype(jnp.bfloat16)
    centre = (jnp.arange(patch, dtype=jnp.float32) + 0.5) / patch
    hann = 0.5 - 0.5 * jnp.cos(2.0 * math.pi * centre)
    window = hann[:, None] * hann[None, :]
    right = jnp.concatenate([cos_tab, sin_tab], axis=1)
    left = jnp.transpose(right)
    return (right, left, window)


def spectra_freq_major(frames, right, left, window):
    box = right.shape[1] // 2
    count = frames.shape[0]
    apodised = (frames.astype(jnp.float32) * window).astype(jnp.bfloat16)
    half = jnp.einsum("nij,jc->nic", apodised, right, preferred_element_type=jnp.float32).astype(
        jnp.bfloat16
    )
    full = jnp.einsum("ki,nic->kcn", left, half, preferred_element_type=jnp.float32)
    real_part = full[:box, :box] - full[box:, box:]
    imag_part = full[:box, box:] + full[box:, :box]
    spec = jnp.stack([real_part, imag_part], axis=2).astype(jnp.bfloat16)
    return spec.reshape(box * box, 2 * count)


def local(tiles, dest_owner, dest_slot, triples):
    frames = tiles[0]
    count = frames.shape[0]
    patch = frames.shape[-1]
    groups = lax.axis_size("grp")
    peers = lax.axis_size("sub")
    target = dest_owner[0] * OWN + dest_slot[0]
    right, left, window = make_tables(patch, BOX)
    spec = spectra_freq_major(frames, right, left, window)
    picked = [jnp.take(spec, triples[w], axis=0).astype(jnp.float32) for w in range(3)]
    ntri = triples.shape[1]
    first, second, third = [p.reshape(ntri, 2, count) for p in picked]
    prod_real = first[:, 0] * second[:, 0] - first[:, 1] * second[:, 1]
    prod_imag = first[:, 0] * second[:, 1] + first[:, 1] * second[:, 0]
    out_real = prod_real * third[:, 0] + prod_imag * third[:, 1]
    out_imag = prod_imag * third[:, 0] - prod_real * third[:, 1]
    terms = jnp.stack([out_real, out_imag], axis=1)
    block = ntri // groups
    terms = terms.reshape(groups, block, 2, count)
    marks = jnp.broadcast_to(target.astype(jnp.float32)[None, None, None, :], (groups, 8, 2, count))
    payload = jnp.concatenate([terms, marks], axis=1)
    got = lax.all_to_all(payload, "grp", split_axis=0, concat_axis=0, tiled=True)
    got_terms = got[:, :block]
    got_marks = got[:, block, 0, :].astype(jnp.int32)
    rows = peers * OWN
    onehot = (
        got_marks[None, :, :] == jnp.arange(rows, dtype=jnp.int32)[:, None, None]
    ).astype(jnp.float32)
    partial_value = jnp.einsum(
        "rgn,gtcn->rct", onehot, got_terms, precision=lax.Precision.HIGHEST
    )
    shaped = partial_value.reshape(peers, OWN, 2, block)
    gathered = lax.all_to_all(shaped, "sub", split_axis=0, concat_axis=0, tiled=True)
    return jnp.sum(gathered, axis=0)


def solution(mesh):
    in_specs = (P("grp", "sub", None, None), P("grp", "sub"), P("grp", "sub"), P())
    out_specs = P("sub", None, "grp")
    return jax.shard_map(local, mesh=mesh, in_specs=in_specs, out_specs=out_specs, check_vma=False)
```

```python
import math

import jax
import jax.numpy as jnp
from jax import lax
from jax.sharding import PartitionSpec as P

BOX = 64
OWN = 8


def make_tables(patch, box):
    rows = jnp.arange(patch, dtype=jnp.int32)[:, None]
    cols = jnp.arange(box, dtype=jnp.int32)[None, :] - box // 2 + patch
    phase = rows * cols % patch
    angle = 2.0 * math.pi * phase.astype(jnp.float32) / patch
    scale = 1.0 / math.sqrt(patch)
    cos_tab = (jnp.cos(angle) * scale).astype(jnp.bfloat16)
    sin_tab = (-jnp.sin(angle) * scale).astype(jnp.bfloat16)
    centre = (jnp.arange(patch, dtype=jnp.float32) + 0.5) / patch
    hann = 0.5 - 0.5 * jnp.cos(2.0 * math.pi * centre)
    window = hann[:, None] * hann[None, :]
    right = jnp.concatenate([cos_tab, sin_tab], axis=1)
    left = jnp.transpose(right)
    return (right, left, window)


def spectra_freq_major(frames, right, left, window):
    box = right.shape[1] // 2
    count = frames.shape[0]
    apodised = (frames.astype(jnp.float32) * window).astype(jnp.bfloat16)
    half = jnp.einsum("nij,jc->nic", apodised, right, preferred_element_type=jnp.float32).astype(
        jnp.bfloat16
    )
    full = jnp.einsum("ki,nic->kcn", left, half, preferred_element_type=jnp.float32)
    real_part = full[:box, :box] - full[box:, box:]
    imag_part = full[:box, box:] + full[box:, :box]
    spec = jnp.stack([real_part, imag_part], axis=2).astype(jnp.bfloat16)
    return spec.reshape(box * box, 2 * count)


def local(tiles, dest_owner, dest_slot, triples):
    frames = tiles[0]
    count = frames.shape[0]
    patch = frames.shape[-1]
    groups = lax.axis_size("grp")
    peers = lax.axis_size("sub")
    target = dest_owner[0] * OWN + dest_slot[0]
    right, left, window = make_tables(patch, BOX)
    spec = spectra_freq_major(frames, right, left, window)
    picked = [jnp.take(spec, triples[w], axis=0).astype(jnp.float32) for w in range(3)]
    ntri = triples.shape[1]
    first, second, third = [p.reshape(ntri, 2, count) for p in picked]
    prod_real = first[:, 0] * second[:, 0] - first[:, 1] * second[:, 1]
    prod_imag = first[:, 0] * second[:, 1] + first[:, 1] * second[:, 0]
    out_real = prod_real * third[:, 0] + prod_imag * third[:, 1]
    out_imag = prod_imag * third[:, 0] - prod_real * third[:, 1]
    terms = jnp.stack([out_real, out_imag], axis=1).astype(jnp.bfloat16)
    block = ntri // groups
    terms = terms.reshape(groups, block, 2, count)
    label = jnp.stack([dest_owner[0], dest_slot[0]]).astype(jnp.bfloat16)
    marks = jnp.broadcast_to(label[None, None, :, :], (groups, 16, 2, count))
    payload = jnp.concatenate([terms, marks], axis=1)
    got = lax.all_to_all(payload, "grp", split_axis=0, concat_axis=0, tiled=True)
    got_terms = got[:, :block]
    got_label = got[:, block].astype(jnp.int32)
    got_marks = got_label[:, 0, :] * OWN + got_label[:, 1, :]
    rows = peers * OWN
    onehot = (
        got_marks[None, :, :] == jnp.arange(rows, dtype=jnp.int32)[:, None, None]
    ).astype(jnp.bfloat16)
    partial_value = jnp.einsum(
        "rgn,gtcn->rct", onehot, got_terms, preferred_element_type=jnp.float32
    )
    shaped = partial_value.astype(jnp.bfloat16).reshape(peers, OWN, 2, block)
    gathered = lax.all_to_all(shaped, "sub", split_axis=0, concat_axis=0, tiled=True)
    return jnp.sum(gathered.astype(jnp.float32), axis=0)


def solution(mesh):
    in_specs = (P("grp", "sub", None, None), P("grp", "sub"), P("grp", "sub"), P())
    out_specs = P("sub", None, "grp")
    return jax.shard_map(local, mesh=mesh, in_specs=in_specs, out_specs=out_specs, check_vma=False)
```

```python
import math

import jax
import jax.numpy as jnp
from jax import lax
from jax.sharding import PartitionSpec as P

BOX = 64
OWN = 8


def make_tables(patch, box):
    rows = jnp.arange(patch, dtype=jnp.int32)[:, None]
    cols = jnp.arange(box, dtype=jnp.int32)[None, :] - box // 2 + patch
    phase = rows * cols % patch
    angle = 2.0 * math.pi * phase.astype(jnp.float32) / patch
    scale = 1.0 / math.sqrt(patch)
    cos_tab = (jnp.cos(angle) * scale).astype(jnp.bfloat16)
    sin_tab = (-jnp.sin(angle) * scale).astype(jnp.bfloat16)
    centre = (jnp.arange(patch, dtype=jnp.float32) + 0.5) / patch
    hann = 0.5 - 0.5 * jnp.cos(2.0 * math.pi * centre)
    window = hann[:, None] * hann[None, :]
    right = jnp.concatenate([cos_tab, sin_tab], axis=1)
    left = jnp.transpose(right)
    return (right, left, window)


def rotation_tables(right):
    box = right.shape[1] // 2
    cos_t = jnp.transpose(right[:, :box])
    sin_t = jnp.transpose(right[:, box:])
    real_rows = jnp.stack([cos_t, -sin_t], axis=1)
    imag_rows = jnp.stack([sin_t, cos_t], axis=1)
    return jnp.stack([real_rows, imag_rows], axis=0)


def spectra_tile_major(frames, right, window):
    box = right.shape[1] // 2
    count, patch = frames.shape[0], frames.shape[1]
    apodised = (frames.astype(jnp.float32) * window).astype(jnp.bfloat16)
    half = jnp.einsum("nij,jc->nic", apodised, right, preferred_element_type=jnp.float32).astype(
        jnp.bfloat16
    )
    halves = half.reshape(count, patch, 2, box)
    spec = jnp.einsum(
        "pjqi,niqk->pjkn", rotation_tables(right), halves, preferred_element_type=jnp.float32
    ).astype(jnp.bfloat16)
    return jnp.transpose(spec, (0, 3, 1, 2)).reshape(2 * count, box * box)


def local(tiles, dest_owner, dest_slot, triples):
    frames = tiles[0]
    count = frames.shape[0]
    patch = frames.shape[-1]
    groups = lax.axis_size("grp")
    peers = lax.axis_size("sub")
    target = dest_owner[0] * OWN + dest_slot[0]
    right, left, window = make_tables(patch, BOX)
    spec = spectra_tile_major(frames, right, window)
    freq_ids = jnp.arange(spec.shape[1], dtype=jnp.int32)[:, None]
    picked = []
    for which in range(3):
        select = (freq_ids == triples[which][None, :]).astype(jnp.bfloat16)
        picked.append(jnp.transpose(jnp.dot(spec, select, preferred_element_type=jnp.float32)))
    ntri = triples.shape[1]
    first, second, third = [p.reshape(ntri, 2, count) for p in picked]
    prod_real = first[:, 0] * second[:, 0] - first[:, 1] * second[:, 1]
    prod_imag = first[:, 0] * second[:, 1] + first[:, 1] * second[:, 0]
    out_real = prod_real * third[:, 0] + prod_imag * third[:, 1]
    out_imag = prod_imag * third[:, 0] - prod_real * third[:, 1]
    terms = jnp.stack([out_real, out_imag], axis=1).astype(jnp.bfloat16)
    block = ntri // groups
    terms = terms.reshape(groups, block, 2, count)
    label = jnp.stack([dest_owner[0], dest_slot[0]]).astype(jnp.bfloat16)
    marks = jnp.broadcast_to(label[None, None, :, :], (groups, 16, 2, count))
    payload = jnp.concatenate([terms, marks], axis=1)
    got = lax.all_to_all(payload, "grp", split_axis=0, concat_axis=0, tiled=True)
    got_terms = got[:, :block]
    got_label = got[:, block].astype(jnp.int32)
    got_marks = got_label[:, 0, :] * OWN + got_label[:, 1, :]
    rows = peers * OWN
    onehot = (
        got_marks[None, :, :] == jnp.arange(rows, dtype=jnp.int32)[:, None, None]
    ).astype(jnp.bfloat16)
    partial_value = jnp.einsum(
        "rgn,gtcn->rct", onehot, got_terms, preferred_element_type=jnp.float32
    )
    shaped = partial_value.astype(jnp.bfloat16).reshape(peers, OWN, 2, block)
    gathered = lax.all_to_all(shaped, "sub", split_axis=0, concat_axis=0, tiled=True)
    return jnp.sum(gathered.astype(jnp.float32), axis=0)


def solution(mesh):
    in_specs = (P("grp", "sub", None, None), P("grp", "sub"), P("grp", "sub"), P())
    out_specs = P("sub", None, "grp")
    return jax.shard_map(local, mesh=mesh, in_specs=in_specs, out_specs=out_specs, check_vma=False)
```

```python
import math

import jax
import jax.numpy as jnp
from jax import lax
from jax.sharding import PartitionSpec as P

BOX = 64
OWN = 8


def make_tables(patch, box):
    rows = jnp.arange(patch, dtype=jnp.int32)[:, None]
    cols = jnp.arange(box, dtype=jnp.int32)[None, :] - box // 2 + patch
    phase = rows * cols % patch
    angle = 2.0 * math.pi * phase.astype(jnp.float32) / patch
    scale = 1.0 / math.sqrt(patch)
    cos_tab = (jnp.cos(angle) * scale).astype(jnp.bfloat16)
    sin_tab = (-jnp.sin(angle) * scale).astype(jnp.bfloat16)
    centre = (jnp.arange(patch, dtype=jnp.float32) + 0.5) / patch
    hann = 0.5 - 0.5 * jnp.cos(2.0 * math.pi * centre)
    window = hann[:, None] * hann[None, :]
    right = jnp.concatenate([cos_tab, sin_tab], axis=1)
    left = jnp.transpose(right)
    return (right, left, window)


def rotation_tables(right):
    box = right.shape[1] // 2
    cos_t = jnp.transpose(right[:, :box])
    sin_t = jnp.transpose(right[:, box:])
    real_rows = jnp.stack([cos_t, -sin_t], axis=1)
    imag_rows = jnp.stack([sin_t, cos_t], axis=1)
    return jnp.stack([real_rows, imag_rows], axis=0)


def spectra_tile_major(frames, right, window):
    box = right.shape[1] // 2
    count, patch = frames.shape[0], frames.shape[1]
    apodised = (frames.astype(jnp.float32) * window).astype(jnp.bfloat16)
    half = jnp.einsum("nij,jc->nic", apodised, right, preferred_element_type=jnp.float32).astype(
        jnp.bfloat16
    )
    halves = half.reshape(count, patch, 2, box)
    spec = jnp.einsum(
        "pjqi,niqk->pjkn", rotation_tables(right), halves, preferred_element_type=jnp.float32
    ).astype(jnp.bfloat16)
    return jnp.transpose(spec, (0, 3, 1, 2)).reshape(2 * count, box * box)


def local(tiles, dest_owner, dest_slot, triples):
    frames = tiles[0]
    count = frames.shape[0]
    patch = frames.shape[-1]
    groups = lax.axis_size("grp")
    peers = lax.axis_size("sub")
    target = dest_owner[0] * OWN + dest_slot[0]
    right, left, window = make_tables(patch, BOX)
    spec = spectra_tile_major(frames, right, window)
    freq_ids = jnp.arange(spec.shape[1], dtype=jnp.int16)[:, None]
    one = jnp.ones((), jnp.bfloat16)
    zero = jnp.zeros((), jnp.bfloat16)
    picked = []
    for which in range(3):
        hit = freq_ids == triples[which].astype(jnp.int16)[None, :]
        select = jnp.where(hit, one, zero)
        picked.append(jnp.transpose(jnp.dot(spec, select, preferred_element_type=jnp.float32)))
    ntri = triples.shape[1]
    first, second, third = [p.reshape(ntri, 2, count) for p in picked]
    prod_real = first[:, 0] * second[:, 0] - first[:, 1] * second[:, 1]
    prod_imag = first[:, 0] * second[:, 1] + first[:, 1] * second[:, 0]
    out_real = prod_real * third[:, 0] + prod_imag * third[:, 1]
    out_imag = prod_imag * third[:, 0] - prod_real * third[:, 1]
    terms = jnp.stack([out_real, out_imag], axis=1).astype(jnp.bfloat16)
    block = ntri // groups
    terms = terms.reshape(groups, block, 2, count)
    label = jnp.stack([dest_owner[0], dest_slot[0]]).astype(jnp.bfloat16)
    marks = jnp.broadcast_to(label[None, None, :, :], (groups, 16, 2, count))
    payload = jnp.concatenate([terms, marks], axis=1)
    got = lax.all_to_all(payload, "grp", split_axis=0, concat_axis=0, tiled=True)
    got_terms = got[:, :block]
    got_label = got[:, block].astype(jnp.int32)
    got_marks = got_label[:, 0, :] * OWN + got_label[:, 1, :]
    rows = peers * OWN
    onehot = (
        got_marks[None, :, :] == jnp.arange(rows, dtype=jnp.int32)[:, None, None]
    ).astype(jnp.bfloat16)
    partial_value = jnp.einsum(
        "rgn,gtcn->rct", onehot, got_terms, preferred_element_type=jnp.float32
    )
    shaped = partial_value.astype(jnp.bfloat16).reshape(peers, OWN, 2, block)
    gathered = lax.all_to_all(shaped, "sub", split_axis=0, concat_axis=0, tiled=True)
    return jnp.sum(gathered.astype(jnp.float32), axis=0)


def solution(mesh):
    in_specs = (P("grp", "sub", None, None), P("grp", "sub"), P("grp", "sub"), P())
    out_specs = P("sub", None, "grp")
    return jax.shard_map(local, mesh=mesh, in_specs=in_specs, out_specs=out_specs, check_vma=False)
```

```python
import math

import jax
import jax.numpy as jnp
from jax import lax
from jax.experimental import pallas as pl
from jax.experimental.pallas import tpu as pltpu
from jax.sharding import PartitionSpec as P

BOX = 64
OWN = 8


def make_tables(patch, box):
    rows = jnp.arange(patch, dtype=jnp.int32)[:, None]
    cols = jnp.arange(box, dtype=jnp.int32)[None, :] - box // 2 + patch
    phase = rows * cols % patch
    angle = 2.0 * math.pi * phase.astype(jnp.float32) / patch
    scale = 1.0 / math.sqrt(patch)
    cos_tab = (jnp.cos(angle) * scale).astype(jnp.bfloat16)
    sin_tab = (-jnp.sin(angle) * scale).astype(jnp.bfloat16)
    centre = (jnp.arange(patch, dtype=jnp.float32) + 0.5) / patch
    hann = 0.5 - 0.5 * jnp.cos(2.0 * math.pi * centre)
    window = hann[:, None] * hann[None, :]
    right = jnp.concatenate([cos_tab, sin_tab], axis=1)
    left = jnp.transpose(right)
    return (right, left, window)


def rotation_tables(right):
    box = right.shape[1] // 2
    cos_t = jnp.transpose(right[:, :box])
    sin_t = jnp.transpose(right[:, box:])
    real_rows = jnp.stack([cos_t, -sin_t], axis=1)
    imag_rows = jnp.stack([sin_t, cos_t], axis=1)
    return jnp.stack([real_rows, imag_rows], axis=0)


def spectra_tile_major(frames, right, window):
    box = right.shape[1] // 2
    count, patch = frames.shape[0], frames.shape[1]
    apodised = (frames.astype(jnp.float32) * window).astype(jnp.bfloat16)
    half = jnp.einsum("nij,jc->nic", apodised, right, preferred_element_type=jnp.float32).astype(
        jnp.bfloat16
    )
    halves = half.reshape(count, patch, 2, box)
    spec = jnp.einsum(
        "pjqi,niqk->jpnk", rotation_tables(right), halves, preferred_element_type=jnp.float32
    ).astype(jnp.bfloat16)
    return flatten_rows(spec)


def flatten_kernel(x_ref, o_ref):
    rows = x_ref.shape[1] * x_ref.shape[2]
    width = x_ref.shape[3]
    for pair in range(x_ref.shape[0] // 2):
        lo = x_ref[2 * pair].reshape(rows, width)
        hi = x_ref[2 * pair + 1].reshape(rows, width)
        o_ref[:, pair * 2 * width : (pair + 1) * 2 * width] = jnp.concatenate([lo, hi], axis=1)


def flatten_rows(spec):
    j1, parts, count, j2 = spec.shape
    size = spec.size * spec.dtype.itemsize
    return pl.pallas_call(
        flatten_kernel,
        out_shape=jax.ShapeDtypeStruct((parts * count, j1 * j2), spec.dtype),
        in_specs=[pl.BlockSpec(memory_space=pltpu.VMEM)],
        out_specs=pl.BlockSpec(memory_space=pltpu.VMEM),
        cost_estimate=pl.CostEstimate(flops=0, transcendentals=0, bytes_accessed=2 * size),
    )(spec)


def local(tiles, dest_owner, dest_slot, triples):
    frames = tiles[0]
    count = frames.shape[0]
    patch = frames.shape[-1]
    groups = lax.axis_size("grp")
    peers = lax.axis_size("sub")
    target = dest_owner[0] * OWN + dest_slot[0]
    right, left, window = make_tables(patch, BOX)
    spec = spectra_tile_major(frames, right, window)
    freq_ids = jnp.arange(spec.shape[1], dtype=jnp.int16)[:, None]
    one = jnp.ones((), jnp.bfloat16)
    zero = jnp.zeros((), jnp.bfloat16)
    picked = []
    for which in range(3):
        hit = freq_ids == triples[which].astype(jnp.int16)[None, :]
        select = jnp.where(hit, one, zero)
        picked.append(jnp.transpose(jnp.dot(spec, select, preferred_element_type=jnp.float32)))
    ntri = triples.shape[1]
    first, second, third = [p.reshape(ntri, 2, count) for p in picked]
    prod_real = first[:, 0] * second[:, 0] - first[:, 1] * second[:, 1]
    prod_imag = first[:, 0] * second[:, 1] + first[:, 1] * second[:, 0]
    out_real = prod_real * third[:, 0] + prod_imag * third[:, 1]
    out_imag = prod_imag * third[:, 0] - prod_real * third[:, 1]
    terms = jnp.stack([out_real, out_imag], axis=1).astype(jnp.bfloat16)
    block = ntri // groups
    terms = terms.reshape(groups, block, 2, count)
    label = jnp.stack([dest_owner[0], dest_slot[0]]).astype(jnp.bfloat16)
    marks = jnp.broadcast_to(label[None, None, :, :], (groups, 16, 2, count))
    payload = jnp.concatenate([terms, marks], axis=1)
    got = lax.all_to_all(payload, "grp", split_axis=0, concat_axis=0, tiled=True)
    got_terms = got[:, :block]
    got_label = got[:, block].astype(jnp.int32)
    got_marks = got_label[:, 0, :] * OWN + got_label[:, 1, :]
    rows = peers * OWN
    onehot = (
        got_marks[None, :, :] == jnp.arange(rows, dtype=jnp.int32)[:, None, None]
    ).astype(jnp.bfloat16)
    partial_value = jnp.einsum(
        "rgn,gtcn->rct", onehot, got_terms, preferred_element_type=jnp.float32
    )
    shaped = partial_value.astype(jnp.bfloat16).reshape(peers, OWN, 2, block)
    gathered = lax.all_to_all(shaped, "sub", split_axis=0, concat_axis=0, tiled=True)
    return jnp.sum(gathered.astype(jnp.float32), axis=0)


def solution(mesh):
    in_specs = (P("grp", "sub", None, None), P("grp", "sub"), P("grp", "sub"), P())
    out_specs = P("sub", None, "grp")
    return jax.shard_map(local, mesh=mesh, in_specs=in_specs, out_specs=out_specs, check_vma=False)
```

```python
import math

import jax
import jax.numpy as jnp
from jax import lax
from jax.sharding import PartitionSpec as P

BOX = 64
OWN = 8


def make_tables(patch, box):
    rows = jnp.arange(patch, dtype=jnp.int32)[:, None]
    cols = jnp.arange(box, dtype=jnp.int32)[None, :] - box // 2 + patch
    phase = rows * cols % patch
    angle = 2.0 * math.pi * phase.astype(jnp.float32) / patch
    scale = 1.0 / math.sqrt(patch)
    cos_tab = (jnp.cos(angle) * scale).astype(jnp.bfloat16)
    sin_tab = (-jnp.sin(angle) * scale).astype(jnp.bfloat16)
    centre = (jnp.arange(patch, dtype=jnp.float32) + 0.5) / patch
    hann = 0.5 - 0.5 * jnp.cos(2.0 * math.pi * centre)
    window = hann[:, None] * hann[None, :]
    right = jnp.concatenate([cos_tab, sin_tab], axis=1)
    left = jnp.transpose(right)
    return (right, left, window)


def rotation_tables(right):
    box = right.shape[1] // 2
    cos_t = jnp.transpose(right[:, :box])
    sin_t = jnp.transpose(right[:, box:])
    real_rows = jnp.stack([cos_t, -sin_t], axis=1)
    imag_rows = jnp.stack([sin_t, cos_t], axis=1)
    return jnp.stack([real_rows, imag_rows], axis=0)


def spectra_tile_major(frames, right, window):
    box = right.shape[1] // 2
    count, patch = frames.shape[0], frames.shape[1]
    apodised = (frames.astype(jnp.float32) * window).astype(jnp.bfloat16)
    half = jnp.einsum("nij,jc->nic", apodised, right, preferred_element_type=jnp.float32).astype(
        jnp.bfloat16
    )
    halves = half.reshape(count, patch, 2, box)
    spec = jnp.einsum(
        "pjqi,niqk->npkj", rotation_tables(right), halves, preferred_element_type=jnp.float32
    ).astype(jnp.bfloat16)
    return spec.reshape(count * 2, box * box)


def local(tiles, dest_owner, dest_slot, triples):
    frames = tiles[0]
    count = frames.shape[0]
    patch = frames.shape[-1]
    groups = lax.axis_size("grp")
    peers = lax.axis_size("sub")
    target = dest_owner[0] * OWN + dest_slot[0]
    right, left, window = make_tables(patch, BOX)
    spec = spectra_tile_major(frames, right, window)
    freq_ids = jnp.arange(spec.shape[1], dtype=jnp.int16)[:, None]
    one = jnp.ones((), jnp.bfloat16)
    zero = jnp.zeros((), jnp.bfloat16)
    picked = []
    swapped = (triples % BOX) * BOX + triples // BOX
    for which in range(3):
        hit = freq_ids == swapped[which].astype(jnp.int16)[None, :]
        select = jnp.where(hit, one, zero)
        picked.append(jnp.transpose(jnp.dot(spec, select, preferred_element_type=jnp.float32)))
    ntri = triples.shape[1]
    first, second, third = [p.reshape(ntri, count, 2) for p in picked]
    prod_real = first[..., 0] * second[..., 0] - first[..., 1] * second[..., 1]
    prod_imag = first[..., 0] * second[..., 1] + first[..., 1] * second[..., 0]
    out_real = prod_real * third[..., 0] + prod_imag * third[..., 1]
    out_imag = prod_imag * third[..., 0] - prod_real * third[..., 1]
    terms = jnp.stack([out_real, out_imag], axis=1).astype(jnp.bfloat16)
    block = ntri // groups
    terms = terms.reshape(groups, block, 2, count)
    label = jnp.stack([dest_owner[0], dest_slot[0]]).astype(jnp.bfloat16)
    marks = jnp.broadcast_to(label[None, None, :, :], (groups, 16, 2, count))
    payload = jnp.concatenate([terms, marks], axis=1)
    got = lax.all_to_all(payload, "grp", split_axis=0, concat_axis=0, tiled=True)
    got_terms = got[:, :block]
    got_label = got[:, block].astype(jnp.int32)
    got_marks = got_label[:, 0, :] * OWN + got_label[:, 1, :]
    rows = peers * OWN
    onehot = (
        got_marks[None, :, :] == jnp.arange(rows, dtype=jnp.int32)[:, None, None]
    ).astype(jnp.bfloat16)
    partial_value = jnp.einsum(
        "rgn,gtcn->rct", onehot, got_terms, preferred_element_type=jnp.float32
    )
    shaped = partial_value.astype(jnp.bfloat16).reshape(peers, OWN, 2, block)
    gathered = lax.all_to_all(shaped, "sub", split_axis=0, concat_axis=0, tiled=True)
    return jnp.sum(gathered.astype(jnp.float32), axis=0)


def solution(mesh):
    in_specs = (P("grp", "sub", None, None), P("grp", "sub"), P("grp", "sub"), P())
    out_specs = P("sub", None, "grp")
    return jax.shard_map(local, mesh=mesh, in_specs=in_specs, out_specs=out_specs, check_vma=False)
```

```python
import math

import jax
import jax.numpy as jnp
from jax import lax
from jax.sharding import PartitionSpec as P

BOX = 64
OWN = 8


def make_tables(patch, box):
    rows = jnp.arange(patch, dtype=jnp.int32)[:, None]
    cols = jnp.arange(box, dtype=jnp.int32)[None, :] - box // 2 + patch
    phase = rows * cols % patch
    angle = 2.0 * math.pi * phase.astype(jnp.float32) / patch
    scale = 1.0 / math.sqrt(patch)
    cos_tab = (jnp.cos(angle) * scale).astype(jnp.bfloat16)
    sin_tab = (-jnp.sin(angle) * scale).astype(jnp.bfloat16)
    centre = (jnp.arange(patch, dtype=jnp.float32) + 0.5) / patch
    hann = 0.5 - 0.5 * jnp.cos(2.0 * math.pi * centre)
    window = hann[:, None] * hann[None, :]
    right = jnp.concatenate([cos_tab, sin_tab], axis=1)
    left = jnp.transpose(right)
    return (right, left, window)


def rotation_tables(right):
    box = right.shape[1] // 2
    cos_t = jnp.transpose(right[:, :box])
    sin_t = jnp.transpose(right[:, box:])
    real_rows = jnp.stack([cos_t, -sin_t], axis=1)
    imag_rows = jnp.stack([sin_t, cos_t], axis=1)
    return jnp.stack([real_rows, imag_rows], axis=0)


def spectra_tile_major(frames, right, window):
    box = right.shape[1] // 2
    count, patch = frames.shape[0], frames.shape[1]
    apodised = (frames.astype(jnp.float32) * window).astype(jnp.bfloat16)
    half = jnp.einsum("nij,jc->nic", apodised, right, preferred_element_type=jnp.float32).astype(
        jnp.bfloat16
    )
    halves = half.reshape(count, patch, 2, box)
    spec = jnp.einsum(
        "pjqi,niqk->npkj", rotation_tables(right), halves, preferred_element_type=jnp.float32
    ).astype(jnp.bfloat16)
    return spec.reshape(count * 2, box * box)


def local(tiles, dest_owner, dest_slot, triples):
    frames = tiles[0]
    count = frames.shape[0]
    patch = frames.shape[-1]
    groups = lax.axis_size("grp")
    peers = lax.axis_size("sub")
    right, left, window = make_tables(patch, BOX)
    spec = spectra_tile_major(frames, right, window)
    freq_ids = jnp.arange(spec.shape[1], dtype=jnp.int16)[:, None]
    one = jnp.ones((), jnp.bfloat16)
    zero = jnp.zeros((), jnp.bfloat16)
    picked = []
    swapped = (triples % BOX) * BOX + triples // BOX
    for which in range(3):
        hit = freq_ids == swapped[which].astype(jnp.int16)[None, :]
        select = jnp.where(hit, one, zero)
        picked.append(jnp.dot(spec, select, preferred_element_type=jnp.float32))
    ntri = triples.shape[1]
    first, second, third = [p.reshape(count, 2, ntri) for p in picked]
    prod_real = first[:, 0] * second[:, 0] - first[:, 1] * second[:, 1]
    prod_imag = first[:, 0] * second[:, 1] + first[:, 1] * second[:, 0]
    out_real = prod_real * third[:, 0] + prod_imag * third[:, 1]
    out_imag = prod_imag * third[:, 0] - prod_real * third[:, 1]
    terms = jnp.stack([out_real, out_imag], axis=0).astype(jnp.bfloat16)
    block = ntri // groups
    terms = jnp.transpose(terms.reshape(2, count, groups, block), (2, 0, 1, 3))
    label = jnp.concatenate([dest_owner[0], dest_slot[0]]).astype(jnp.bfloat16)
    marks = jnp.broadcast_to(label[None, None, None, :], (groups, 2, 8, 2 * count))
    payload = jnp.concatenate([terms, marks], axis=2)
    got = lax.all_to_all(payload, "grp", split_axis=0, concat_axis=0, tiled=True)
    got_terms = got[:, :, :count]
    got_label = got[:, 0, count].astype(jnp.int32)
    got_marks = got_label[:, :count] * OWN + got_label[:, count:]
    rows = peers * OWN
    onehot = (
        got_marks[None, :, :] == jnp.arange(rows, dtype=jnp.int32)[:, None, None]
    ).astype(jnp.bfloat16)
    partial_value = jnp.einsum(
        "rgn,gcnt->rct", onehot, got_terms, preferred_element_type=jnp.float32
    )
    shaped = partial_value.astype(jnp.bfloat16).reshape(peers, OWN, 2, block)
    gathered = lax.all_to_all(shaped, "sub", split_axis=0, concat_axis=0, tiled=True)
    return jnp.sum(gathered.astype(jnp.float32), axis=0)


def solution(mesh):
    in_specs = (P("grp", "sub", None, None), P("grp", "sub"), P("grp", "sub"), P())
    out_specs = P("sub", None, "grp")
    return jax.shard_map(local, mesh=mesh, in_specs=in_specs, out_specs=out_specs, check_vma=False)
```

```python
import math

import jax
import jax.numpy as jnp
from jax import lax
from jax.sharding import PartitionSpec as P

BOX = 64
OWN = 8


def make_tables(patch, box):
    rows = jnp.arange(patch, dtype=jnp.int32)[:, None]
    cols = jnp.arange(box, dtype=jnp.int32)[None, :] - box // 2 + patch
    phase = rows * cols % patch
    angle = 2.0 * math.pi * phase.astype(jnp.float32) / patch
    scale = 1.0 / math.sqrt(patch)
    cos_tab = (jnp.cos(angle) * scale).astype(jnp.bfloat16)
    sin_tab = (-jnp.sin(angle) * scale).astype(jnp.bfloat16)
    centre = (jnp.arange(patch, dtype=jnp.float32) + 0.5) / patch
    hann = 0.5 - 0.5 * jnp.cos(2.0 * math.pi * centre)
    window = hann[:, None] * hann[None, :]
    right = jnp.concatenate([cos_tab, sin_tab], axis=1)
    left = jnp.transpose(right)
    return (right, left, window)


def rotation_tables(right):
    box = right.shape[1] // 2
    cos_t = jnp.transpose(right[:, :box])
    sin_t = jnp.transpose(right[:, box:])
    real_rows = jnp.stack([cos_t, -sin_t], axis=1)
    imag_rows = jnp.stack([sin_t, cos_t], axis=1)
    return jnp.stack([real_rows, imag_rows], axis=0)


def spectra_tile_major(frames, right, window):
    box = right.shape[1] // 2
    count, patch = frames.shape[0], frames.shape[1]
    apodised = (frames.astype(jnp.float32) * window).astype(jnp.bfloat16)
    half = jnp.einsum("nij,jc->nic", apodised, right, preferred_element_type=jnp.float32).astype(
        jnp.bfloat16
    )
    halves = half.reshape(count, patch, 2, box)
    spec = jnp.einsum(
        "pjqi,niqk->npkj", rotation_tables(right), halves, preferred_element_type=jnp.float32
    ).astype(jnp.bfloat16)
    return spec.reshape(count * 2, box, box)


def local(tiles, dest_owner, dest_slot, triples):
    frames = tiles[0]
    count = frames.shape[0]
    patch = frames.shape[-1]
    groups = lax.axis_size("grp")
    peers = lax.axis_size("sub")
    right, left, window = make_tables(patch, BOX)
    spec = spectra_tile_major(frames, right, window)
    axis_ids = jnp.arange(BOX, dtype=jnp.int16)
    freq_ids = (axis_ids[:, None] * BOX + axis_ids[None, :])[:, :, None]
    one = jnp.ones((), jnp.bfloat16)
    zero = jnp.zeros((), jnp.bfloat16)
    picked = []
    swapped = (triples % BOX) * BOX + triples // BOX
    for which in range(3):
        hit = freq_ids == swapped[which].astype(jnp.int16)[None, None, :]
        select = jnp.where(hit, one, zero)
        picked.append(jnp.einsum("rkj,kjt->rt", spec, select, preferred_element_type=jnp.float32))
    ntri = triples.shape[1]
    first, second, third = [p.reshape(count, 2, ntri) for p in picked]
    prod_real = first[:, 0] * second[:, 0] - first[:, 1] * second[:, 1]
    prod_imag = first[:, 0] * second[:, 1] + first[:, 1] * second[:, 0]
    out_real = prod_real * third[:, 0] + prod_imag * third[:, 1]
    out_imag = prod_imag * third[:, 0] - prod_real * third[:, 1]
    terms = jnp.stack([out_real, out_imag], axis=0).astype(jnp.bfloat16)
    block = ntri // groups
    terms = jnp.transpose(terms.reshape(2, count, groups, block), (2, 0, 1, 3))
    label = jnp.concatenate([dest_owner[0], dest_slot[0]]).astype(jnp.bfloat16)
    marks = jnp.broadcast_to(label[None, None, None, :], (groups, 2, 8, 2 * count))
    payload = jnp.concatenate([terms, marks], axis=2)
    got = lax.all_to_all(payload, "grp", split_axis=0, concat_axis=0, tiled=True)
    got_terms = got[:, :, :count]
    got_label = got[:, 0, count].astype(jnp.int32)
    got_marks = got_label[:, :count] * OWN + got_label[:, count:]
    rows = peers * OWN
    onehot = (
        got_marks[None, :, :] == jnp.arange(rows, dtype=jnp.int32)[:, None, None]
    ).astype(jnp.bfloat16)
    partial_value = jnp.einsum(
        "rgn,gcnt->rct", onehot, got_terms, preferred_element_type=jnp.float32
    )
    shaped = partial_value.astype(jnp.bfloat16).reshape(peers, OWN, 2, block)
    gathered = lax.all_to_all(shaped, "sub", split_axis=0, concat_axis=0, tiled=True)
    return jnp.sum(gathered.astype(jnp.float32), axis=0)


def solution(mesh):
    in_specs = (P("grp", "sub", None, None), P("grp", "sub"), P("grp", "sub"), P())
    out_specs = P("sub", None, "grp")
    return jax.shard_map(local, mesh=mesh, in_specs=in_specs, out_specs=out_specs, check_vma=False)
```

```python
import math

import jax
import jax.numpy as jnp
from jax import lax
from jax.sharding import PartitionSpec as P

BOX = 64
OWN = 8


def make_tables(patch, box):
    rows = jnp.arange(patch, dtype=jnp.int32)[:, None]
    cols = jnp.arange(box, dtype=jnp.int32)[None, :] - box // 2 + patch
    phase = rows * cols % patch
    angle = 2.0 * math.pi * phase.astype(jnp.float32) / patch
    scale = 1.0 / math.sqrt(patch)
    cos_tab = (jnp.cos(angle) * scale).astype(jnp.bfloat16)
    sin_tab = (-jnp.sin(angle) * scale).astype(jnp.bfloat16)
    centre = (jnp.arange(patch, dtype=jnp.float32) + 0.5) / patch
    hann = 0.5 - 0.5 * jnp.cos(2.0 * math.pi * centre)
    window = hann[:, None] * hann[None, :]
    right = jnp.concatenate([cos_tab, sin_tab], axis=1)
    left = jnp.transpose(right)
    return (right, left, window)


def rotation_tables(right):
    box = right.shape[1] // 2
    cos_t = jnp.transpose(right[:, :box])
    sin_t = jnp.transpose(right[:, box:])
    real_rows = jnp.stack([cos_t, -sin_t], axis=1)
    imag_rows = jnp.stack([sin_t, cos_t], axis=1)
    return jnp.stack([real_rows, imag_rows], axis=0)


def spectra_tile_major(frames, right, window):
    box = right.shape[1] // 2
    count, patch = frames.shape[0], frames.shape[1]
    apodised = (frames.astype(jnp.float32) * window).astype(jnp.bfloat16)
    half = jnp.einsum("nij,jc->nic", apodised, right, preferred_element_type=jnp.float32).astype(
        jnp.bfloat16
    )
    halves = half.reshape(count, patch, 2, box)
    spec = jnp.einsum(
        "pjqi,niqk->npkj", rotation_tables(right), halves, preferred_element_type=jnp.float32
    ).astype(jnp.bfloat16)
    return spec.reshape(count * 2, box * box)


def local(tiles, dest_owner, dest_slot, triples):
    frames = tiles[0]
    count = frames.shape[0]
    patch = frames.shape[-1]
    groups = lax.axis_size("grp")
    peers = lax.axis_size("sub")
    right, left, window = make_tables(patch, BOX)
    spec = spectra_tile_major(frames, right, window)
    freq_ids = jnp.arange(spec.shape[1], dtype=jnp.int16)[:, None]
    one = jnp.ones((), jnp.bfloat16)
    zero = jnp.zeros((), jnp.bfloat16)
    picked = []
    swapped = (triples % BOX) * BOX + triples // BOX
    for which in range(3):
        hit = freq_ids == swapped[which].astype(jnp.int16)[None, :]
        select = jnp.where(hit, one, zero)
        picked.append(jnp.dot(spec, select, preferred_element_type=jnp.float32))
    ntri = triples.shape[1]
    first, second, third = [p.reshape(count, 2, ntri) for p in picked]
    prod_real = first[:, 0] * second[:, 0] - first[:, 1] * second[:, 1]
    prod_imag = first[:, 0] * second[:, 1] + first[:, 1] * second[:, 0]
    out_real = prod_real * third[:, 0] + prod_imag * third[:, 1]
    out_imag = prod_imag * third[:, 0] - prod_real * third[:, 1]
    terms = jnp.stack([out_real, out_imag], axis=0).astype(jnp.bfloat16)
    block = ntri // groups
    terms = jnp.transpose(terms.reshape(2 * count, groups, block), (1, 0, 2))
    label = jnp.concatenate([dest_owner[0], dest_slot[0]]).astype(jnp.bfloat16)
    marks = jnp.broadcast_to(label[None, None, :], (groups, 8, 2 * count))
    payload = jnp.concatenate([terms, marks], axis=1)
    got = lax.all_to_all(payload, "grp", split_axis=0, concat_axis=0, tiled=True)
    got_terms = got[:, : 2 * count].reshape(groups, 2, count, block)
    got_label = got[:, 2 * count].astype(jnp.int32)
    got_marks = got_label[:, :count] * OWN + got_label[:, count:]
    rows = peers * OWN
    onehot = (
        got_marks[None, :, :] == jnp.arange(rows, dtype=jnp.int32)[:, None, None]
    ).astype(jnp.bfloat16)
    partial_value = jnp.einsum(
        "rgn,gcnt->rct", onehot, got_terms, preferred_element_type=jnp.float32
    )
    shaped = partial_value.astype(jnp.bfloat16).reshape(peers, OWN, 2, block)
    gathered = lax.all_to_all(shaped, "sub", split_axis=0, concat_axis=0, tiled=True)
    return jnp.sum(gathered.astype(jnp.float32), axis=0)


def solution(mesh):
    in_specs = (P("grp", "sub", None, None), P("grp", "sub"), P("grp", "sub"), P())
    out_specs = P("sub", None, "grp")
    return jax.shard_map(local, mesh=mesh, in_specs=in_specs, out_specs=out_specs, check_vma=False)
```

```python
import math

import jax
import jax.numpy as jnp
from jax import lax
from jax.sharding import PartitionSpec as P

BOX = 64
OWN = 8


def make_tables(patch, box):
    rows = jnp.arange(patch, dtype=jnp.int32)[:, None]
    cols = jnp.arange(box, dtype=jnp.int32)[None, :] - box // 2 + patch
    phase = rows * cols % patch
    angle = 2.0 * math.pi * phase.astype(jnp.float32) / patch
    scale = 1.0 / math.sqrt(patch)
    cos_tab = (jnp.cos(angle) * scale).astype(jnp.bfloat16)
    sin_tab = (-jnp.sin(angle) * scale).astype(jnp.bfloat16)
    centre = (jnp.arange(patch, dtype=jnp.float32) + 0.5) / patch
    hann = 0.5 - 0.5 * jnp.cos(2.0 * math.pi * centre)
    window = hann[:, None] * hann[None, :]
    right = jnp.concatenate([cos_tab, sin_tab], axis=1)
    left = jnp.transpose(right)
    return (right, left, window)


def rotation_tables(right):
    box = right.shape[1] // 2
    cos_t = jnp.transpose(right[:, :box])
    sin_t = jnp.transpose(right[:, box:])
    real_rows = jnp.stack([cos_t, -sin_t], axis=1)
    imag_rows = jnp.stack([sin_t, cos_t], axis=1)
    return jnp.stack([real_rows, imag_rows], axis=0)


def spectra_tile_major(frames, right, window):
    box = right.shape[1] // 2
    count, patch = frames.shape[0], frames.shape[1]
    apodised = (frames.astype(jnp.float32) * window).astype(jnp.bfloat16)
    half = jnp.einsum("nij,jc->nic", apodised, right, preferred_element_type=jnp.float32).astype(
        jnp.bfloat16
    )
    halves = half.reshape(count, patch, 2, box)
    spec = jnp.einsum(
        "pjqi,niqk->npkj", rotation_tables(right), halves, preferred_element_type=jnp.float32
    ).astype(jnp.bfloat16)
    return spec.reshape(count * 2, box * box)


def local(tiles, dest_owner, dest_slot, triples):
    frames = tiles[0]
    count = frames.shape[0]
    patch = frames.shape[-1]
    groups = lax.axis_size("grp")
    peers = lax.axis_size("sub")
    right, left, window = make_tables(patch, BOX)
    spec = spectra_tile_major(frames, right, window)
    freq_ids = jnp.arange(spec.shape[1], dtype=jnp.int16)[:, None]
    one = jnp.ones((), jnp.bfloat16)
    zero = jnp.zeros((), jnp.bfloat16)
    swapped = (triples % BOX) * BOX + triples // BOX
    hit = freq_ids == swapped.reshape(1, -1).astype(jnp.int16)
    select = jnp.where(hit, one, zero)
    every = jnp.dot(spec, select, preferred_element_type=jnp.float32)
    ntri = triples.shape[1]
    picked = [every[:, which * ntri : (which + 1) * ntri] for which in range(3)]
    first, second, third = [p.reshape(count, 2, ntri) for p in picked]
    prod_real = first[:, 0] * second[:, 0] - first[:, 1] * second[:, 1]
    prod_imag = first[:, 0] * second[:, 1] + first[:, 1] * second[:, 0]
    out_real = prod_real * third[:, 0] + prod_imag * third[:, 1]
    out_imag = prod_imag * third[:, 0] - prod_real * third[:, 1]
    terms = jnp.stack([out_real, out_imag], axis=0).astype(jnp.bfloat16)
    block = ntri // groups
    terms = jnp.transpose(terms.reshape(2, count, groups, block), (2, 0, 1, 3))
    label = jnp.concatenate([dest_owner[0], dest_slot[0]]).astype(jnp.bfloat16)
    marks = jnp.broadcast_to(label[None, None, None, :], (groups, 2, 8, 2 * count))
    payload = jnp.concatenate([terms, marks], axis=2)
    got = lax.all_to_all(payload, "grp", split_axis=0, concat_axis=0, tiled=True)
    got_terms = got[:, :, :count]
    got_label = got[:, 0, count].astype(jnp.int32)
    got_marks = got_label[:, :count] * OWN + got_label[:, count:]
    rows = peers * OWN
    onehot = (
        got_marks[None, :, :] == jnp.arange(rows, dtype=jnp.int32)[:, None, None]
    ).astype(jnp.bfloat16)
    partial_value = jnp.einsum(
        "rgn,gcnt->rct", onehot, got_terms, preferred_element_type=jnp.float32
    )
    shaped = partial_value.astype(jnp.bfloat16).reshape(peers, OWN, 2, block)
    gathered = lax.all_to_all(shaped, "sub", split_axis=0, concat_axis=0, tiled=True)
    return jnp.sum(gathered.astype(jnp.float32), axis=0)


def solution(mesh):
    in_specs = (P("grp", "sub", None, None), P("grp", "sub"), P("grp", "sub"), P())
    out_specs = P("sub", None, "grp")
    return jax.shard_map(local, mesh=mesh, in_specs=in_specs, out_specs=out_specs, check_vma=False)
```

```python
import math

import jax
import jax.numpy as jnp
from jax import lax
from jax.sharding import PartitionSpec as P

BOX = 64
OWN = 8


def make_tables(patch, box):
    rows = jnp.arange(patch, dtype=jnp.int32)[:, None]
    cols = jnp.arange(box, dtype=jnp.int32)[None, :] - box // 2 + patch
    phase = rows * cols % patch
    angle = 2.0 * math.pi * phase.astype(jnp.float32) / patch
    scale = 1.0 / math.sqrt(patch)
    cos_tab = (jnp.cos(angle) * scale).astype(jnp.bfloat16)
    sin_tab = (-jnp.sin(angle) * scale).astype(jnp.bfloat16)
    centre = (jnp.arange(patch, dtype=jnp.float32) + 0.5) / patch
    hann = 0.5 - 0.5 * jnp.cos(2.0 * math.pi * centre)
    window = hann[:, None] * hann[None, :]
    right = jnp.concatenate([cos_tab, sin_tab], axis=1)
    left = jnp.transpose(right)
    return (right, left, window)


def rotation_tables(right):
    box = right.shape[1] // 2
    cos_t = jnp.transpose(right[:, :box])
    sin_t = jnp.transpose(right[:, box:])
    real_rows = jnp.stack([cos_t, -sin_t], axis=1)
    imag_rows = jnp.stack([sin_t, cos_t], axis=1)
    return jnp.stack([real_rows, imag_rows], axis=0)


def spectra_tile_major(frames, right, window):
    box = right.shape[1] // 2
    count, patch = frames.shape[0], frames.shape[1]
    apodised = (frames.astype(jnp.float32) * window).astype(jnp.bfloat16)
    half = jnp.einsum("nij,jc->nic", apodised, right, preferred_element_type=jnp.float32).astype(
        jnp.bfloat16
    )
    halves = half.reshape(count, patch, 2, box)
    spec = jnp.einsum(
        "pjqi,niqk->npkj", rotation_tables(right), halves, preferred_element_type=jnp.float32
    ).astype(jnp.bfloat16)
    return spec.reshape(count * 2, box * box)


def local(tiles, dest_owner, dest_slot, triples):
    frames = tiles[0]
    count = frames.shape[0]
    patch = frames.shape[-1]
    groups = lax.axis_size("grp")
    peers = lax.axis_size("sub")
    right, left, window = make_tables(patch, BOX)
    spec = spectra_tile_major(frames, right, window)
    freq_ids = jnp.arange(spec.shape[1], dtype=jnp.int16)[:, None]
    one = jnp.ones((), jnp.bfloat16)
    zero = jnp.zeros((), jnp.bfloat16)
    picked = []
    swapped = (triples % BOX) * BOX + triples // BOX
    for which in range(3):
        hit = freq_ids == swapped[which].astype(jnp.int16)[None, :]
        select = jnp.where(hit, one, zero)
        picked.append(jnp.dot(spec, select, preferred_element_type=jnp.float32))
    ntri = triples.shape[1]
    first, second, third = [p.reshape(count, 2, ntri) for p in picked]
    prod_real = first[:, 0] * second[:, 0] - first[:, 1] * second[:, 1]
    prod_imag = first[:, 0] * second[:, 1] + first[:, 1] * second[:, 0]
    out_real = prod_real * third[:, 0] + prod_imag * third[:, 1]
    out_imag = prod_imag * third[:, 0] - prod_real * third[:, 1]
    terms = jnp.stack([out_real, out_imag], axis=0).astype(jnp.bfloat16)
    block = ntri // groups
    terms = jnp.transpose(terms.reshape(2, count, groups, block), (2, 0, 1, 3))
    label = jnp.concatenate([dest_owner[0], dest_slot[0]]).astype(jnp.bfloat16)
    marks = jnp.broadcast_to(label[None, None, None, :], (groups, 2, 8, 2 * count))
    payload = jnp.concatenate([terms, marks], axis=2)
    got = lax.all_to_all(payload, "grp", split_axis=0, concat_axis=0, tiled=True)
    got_terms = got[:, :, :count]
    got_label = got[:, 0, count].astype(jnp.int32)
    got_marks = got_label[:, :count] * OWN + got_label[:, count:]
    rows = peers * OWN
    row_ids = jnp.arange(rows, dtype=jnp.int16)[:, None, None]
    onehot = jnp.where(got_marks.astype(jnp.int16)[None, :, :] == row_ids, one, zero)
    partial_value = jnp.einsum(
        "rgn,gcnt->rct", onehot, got_terms, preferred_element_type=jnp.float32
    )
    shaped = partial_value.astype(jnp.bfloat16).reshape(peers, OWN, 2, block)
    gathered = lax.all_to_all(shaped, "sub", split_axis=0, concat_axis=0, tiled=True)
    return jnp.sum(gathered.astype(jnp.float32), axis=0)


def solution(mesh):
    in_specs = (P("grp", "sub", None, None), P("grp", "sub"), P("grp", "sub"), P())
    out_specs = P("sub", None, "grp")
    return jax.shard_map(local, mesh=mesh, in_specs=in_specs, out_specs=out_specs, check_vma=False)
```
